512 devices in a mesh: seq: 64 (over z, x, core), tp: 8 (over y).
Axes of the slice: x: 4, y: 8, z: 8, core: 2. Of those that a mesh axis runs over, the one named last changes fastest.
Arguments:
- queries: float32 [16384, 4096], P(('seq', 'tp')), may hold values from -8 to 8
- keys: float32 [16384, 2048], P(('seq', 'tp')), may hold values from -8 to 8
- values: float32 [16384, 2048], P(('seq', 'tp')), may hold values from -6 to 6
- out_grad: float32 [16384, 4096], P(('seq', 'tp')), may hold values from -6 to 6
- positions: int32 [16384], P('seq'), may hold values from 0 to 8191, as said below
Outputs:
- attended: float32 [16384, 4096], P(('seq', 'tp'))
- grad_queries: float32 [16384, 4096], P(('seq', 'tp'))
- grad_keys: float32 [16384, 2048], P(('seq', 'tp'))
- grad_values: float32 [16384, 2048], P(('seq', 'tp'))
The draws below stay inside these ranges and needn't reach their ends.
Inputs may be any that keep to these rules, and one draw needn't show every extreme that they name: `positions`: each token's position within its document: one more than the token before, except at a document's first token, where it is 0; the slice's first document may have begun before the slice.
All inputs are finite; a program needn't handle non-finite values.
Results may differ from the reference program's by a relative error of at most 0.0005.
Values sent between devices are 32-bit elements; how exact they have to be, the bound alone decides.
No kernel may reach another device: no remote copies, remote signals or barrier semaphores. Data moves between devices by JAX's collectives and lax.ppermute only.
A program may use at most 64 MiB of HBM per device.

```python
import jax
import jax.numpy as jnp
from jax import lax

HEADS = 32
KV_HEADS = 16
HEAD_DIM = 128
WINDOW = 1024
TOK_DEV = 256
TOKENS = 16384


def base_field(key, width):
    return jnp.clip(jax.random.normal(key, (TOKENS, width, HEAD_DIM), jnp.float32), -8.0, 8.0)


def draw_queries(key, part):
    base = base_field(jax.random.fold_in(key, 1), HEADS)
    return base.reshape(TOKENS, HEADS * HEAD_DIM).astype(jnp.float32)


def draw_keys(key, part):
    base = base_field(jax.random.fold_in(key, 2), KV_HEADS)
    return base.reshape(TOKENS, KV_HEADS * HEAD_DIM).astype(jnp.float32)


def draw_positions(key, part):
    token_index = jnp.arange(TOKENS, dtype=jnp.int32)
    region_count = (TOKENS + 1023) // 1024
    pick = jax.random.randint(jax.random.fold_in(key, 21), (region_count,), 0, 4)
    spacing_table = jnp.array([32, 256, 2048, 16384], jnp.int32)
    spacing = spacing_table[pick][token_index // 1024]
    raw_draw = jax.random.randint(jax.random.fold_in(key, 22), (TOKENS,), 0, 2 ** 30)
    is_start = (raw_draw % spacing == 0) & (token_index < TOKENS // 2)
    is_start = is_start | (token_index == TOKENS // 2) | (token_index == TOKENS // 4)
    is_start = is_start & (token_index > 0)
    doc_start = lax.cummax(jnp.where(is_start, token_index, 0))
    offset = jax.random.randint(jax.random.fold_in(key, 23), (), 0, TOKENS // 4)
    return (token_index - doc_start + jnp.where(doc_start == 0, offset, 0)).astype(jnp.int32)


def steps_of(own_key, extent, cuts, low, largest):
    def one(position, shards_of):
        steps = jax.random.uniform(jax.random.fold_in(jax.random.fold_in(own_key, 6), position), (shards_of,), jnp.float32, low / len(cuts), largest / len(cuts))
        return jnp.repeat(jnp.exp(steps), extent[position] // shards_of).reshape((-1,) + (1,) * (len(extent) - position - 1))

    factor_of = one(*cuts[0])
    for cut in cuts[1:]:
        factor_of = factor_of * one(*cut)
    return factor_of


def centred(own_key, dims, scale, reach, pieces=(), held_as=jnp.bfloat16):
    drawn = scale * jax.random.normal(own_key, dims, jnp.float32)
    if pieces:
        drawn = drawn * steps_of(own_key, dims, pieces, -0.22, 0.18)
    return jnp.clip(drawn, -reach, reach).astype(held_as)


def setup_inputs(seed: int = 0) -> dict:
    splits = jax.random.split(jax.random.key(seed), 6)
    queries = draw_queries(jax.random.fold_in(splits[5], 71), 0)
    keys = draw_keys(jax.random.fold_in(splits[5], 71), 0)
    values = centred(splits[2], (TOKENS, KV_HEADS * HEAD_DIM), 1.0, 6.0, ((0, 512),), jnp.float32)
    out_grad = centred(splits[3], (TOKENS, HEADS * HEAD_DIM), 1.0, 6.0, ((0, 512),), jnp.float32)
    positions = draw_positions(jax.random.fold_in(splits[5], 71), 0)
    return {"queries": queries, "keys": keys, "values": values, "out_grad": out_grad, "positions": positions}


score_scale = 168.0 ** (-0.5)
neg_fill = -1e+30

def reference(queries, keys, values, out_grad, positions):
    total_rows = queries.shape[0]
    group_size = HEADS // KV_HEADS
    token_index = jnp.arange(total_rows, dtype=jnp.int32)
    doc_starts = (token_index - positions.astype(jnp.int32)).astype(jnp.int32)
    padded_starts = jnp.concatenate([jnp.zeros((WINDOW,), jnp.int32), doc_starts])
    block_count = total_rows // TOK_DEV
    precise = lax.Precision.HIGHEST

    def forward(query_all, key_all, value_all):
        padded_keys = jnp.concatenate([jnp.zeros((WINDOW, key_all.shape[1]), key_all.dtype), key_all])
        padded_values = jnp.concatenate([jnp.zeros((WINDOW, value_all.shape[1]), value_all.dtype), value_all])

        def attend_block(block_id):
            block_start = (block_id * TOK_DEV).astype(jnp.int32)
            query_block = lax.dynamic_slice_in_dim(query_all, block_start, TOK_DEV, 0).reshape(TOK_DEV, KV_HEADS, group_size, HEAD_DIM)
            key_block = lax.dynamic_slice_in_dim(padded_keys, block_start, WINDOW + TOK_DEV, 0).reshape(WINDOW + TOK_DEV, KV_HEADS, HEAD_DIM)
            value_block = lax.dynamic_slice_in_dim(padded_values, block_start, WINDOW + TOK_DEV, 0).reshape(WINDOW + TOK_DEV, KV_HEADS, HEAD_DIM)
            query_starts = lax.dynamic_slice_in_dim(doc_starts, block_start, TOK_DEV, 0)
            key_starts = lax.dynamic_slice_in_dim(padded_starts, block_start, WINDOW + TOK_DEV, 0)
            query_index = block_start + jnp.arange(TOK_DEV, dtype=jnp.int32)
            key_index = block_start - WINDOW + jnp.arange(WINDOW + TOK_DEV, dtype=jnp.int32)
            offsets = query_index[:, None] - key_index[None, :]
            visible = (key_index >= 0)[None, :] & (offsets >= 0) & (offsets < WINDOW) & (query_starts[:, None] == key_starts[None, :])
            scores = jnp.einsum('qgrd,kgd->grqk', query_block, key_block, precision=precise) * score_scale
            scores = jnp.where(visible, scores, neg_fill)
            top_score = lax.stop_gradient(lax.optimization_barrier(jnp.max(scores, axis=-1, keepdims=True)))
            weights = jnp.exp(scores - top_score)
            totals = lax.optimization_barrier(jnp.sum(weights, axis=-1))
            mixed = jnp.einsum('grqk,kgd->qgrd', weights, value_block, precision=precise)
            mixed = mixed / jnp.transpose(totals, (2, 0, 1))[..., None]
            return mixed.reshape(TOK_DEV, HEADS * HEAD_DIM)
        results = lax.map(jax.checkpoint(attend_block), jnp.arange(block_count, dtype=jnp.int32))
        return results.reshape(total_rows, HEADS * HEAD_DIM)
    attended, pullback = jax.vjp(forward, queries, keys, values)
    grad_queries, grad_keys, grad_values = pullback(out_grad)
    return (attended, grad_queries, grad_keys, grad_values)
```

```python
import jax
import jax.numpy as jnp
from jax import lax
from jax.sharding import Mesh
from jax.sharding import PartitionSpec as P

HEAD_DIM = 128
WINDOW = 1024


score_scale = 168.0 ** (-0.5)
neg_fill = -1e30

GROUP = ("core", "tp")


def from_behind(block, axis, distance):
    devices = range(lax.axis_size(axis))
    route = [(i - distance, i) for i in devices if i - distance in devices]
    return lax.ppermute(block, axis, route)


def per_device(queries, keys, values, out_grad, positions):
    n_group = lax.axis_size(GROUP)
    tok_dev = queries.shape[0]
    head_dim = HEAD_DIM
    q_cols = queries.shape[1] // n_group
    kv_cols = keys.shape[1] // n_group
    group_size = q_cols // kv_cols
    kv_local = kv_cols // head_dim

    kv_in = jnp.concatenate(
        [keys.reshape(tok_dev, n_group, kv_cols), values.reshape(tok_dev, n_group, kv_cols)], axis=2
    )
    kv_here = lax.all_to_all(kv_in, GROUP, split_axis=1, concat_axis=0, tiled=True)
    kv_here = kv_here.reshape(-1, 2 * kv_cols)
    qg_in = jnp.concatenate(
        [queries.reshape(tok_dev, n_group, q_cols), out_grad.reshape(tok_dev, n_group, q_cols)], axis=2
    )
    qg_here = lax.all_to_all(qg_in, GROUP, split_axis=1, concat_axis=0, tiled=True)
    qg_here = qg_here.reshape(-1, 2 * q_cols)
    query_local = qg_here[:, :q_cols]
    grad_local = qg_here[:, q_cols:]

    tok_rows = kv_here.shape[0]
    reach = -(-WINDOW // tok_rows)
    block = lax.axis_index("chip")
    first_row = block * tok_rows
    all_positions = lax.all_gather(positions, "core", axis=0, tiled=True)
    query_index = first_row + jnp.arange(tok_rows, dtype=jnp.int32)
    own_starts = query_index - all_positions

    earlier = [from_behind(kv_here, "chip", distance) for distance in range(reach, 0, -1)]
    kv_window = jnp.concatenate(earlier + [kv_here], axis=0)
    key_window = kv_window[:, :kv_cols]
    value_window = kv_window[:, kv_cols:]
    key_index = first_row - reach * tok_rows + jnp.arange((reach + 1) * tok_rows, dtype=jnp.int32)
    offsets = query_index[:, None] - key_index[None, :]
    visible = (
        (key_index >= 0)[None, :]
        & (offsets >= 0)
        & (offsets < WINDOW)
        & (key_index[None, :] >= own_starts[:, None])
    )
    precise = lax.Precision.HIGHEST
    query_heads = query_local.reshape(tok_rows, kv_local, group_size, head_dim)
    key_heads = key_window.reshape(-1, kv_local, head_dim)
    value_heads = value_window.reshape(-1, kv_local, head_dim)
    scores = jnp.einsum("qgrd,kgd->grqk", query_heads, key_heads, precision=precise) * score_scale
    scores = jnp.where(visible, scores, neg_fill)
    top_score = jnp.max(scores, axis=-1, keepdims=True)
    weights = jnp.exp(scores - top_score)
    totals = jnp.sum(weights, axis=-1)
    out_heads = jnp.einsum("grqk,kgd->qgrd", weights, value_heads, precision=precise)
    out_heads = out_heads / jnp.transpose(totals, (2, 0, 1))[..., None]
    attn_probs = weights / totals[..., None]
    grad_heads = grad_local.reshape(tok_rows, kv_local, group_size, head_dim)
    deltas = jnp.transpose(jnp.sum(grad_heads * out_heads, axis=-1), (1, 2, 0))
    grad_probs = jnp.einsum("qgrd,kgd->grqk", grad_heads, value_heads, precision=precise)
    grad_scores = attn_probs * (grad_probs - deltas[..., None])
    grad_query = (
        jnp.einsum("grqk,kgd->qgrd", grad_scores, key_heads, precision=precise) * score_scale
    )
    key_grads = (
        jnp.einsum("grqk,qgrd->kgd", grad_scores, query_heads, precision=precise) * score_scale
    ).reshape(-1, kv_cols)
    value_grads = jnp.einsum("grqk,qgrd->kgd", attn_probs, grad_heads, precision=precise).reshape(
        -1, kv_cols
    )
    kv_grads = jnp.concatenate([key_grads, value_grads], axis=1)

    def window_block(distance):
        begin = (reach - distance) * tok_rows
        return kv_grads[begin : begin + tok_rows]

    kv_total = window_block(0)
    for distance in range(1, reach + 1):
        kv_total = kv_total + from_behind(window_block(distance), "chip", -distance)

    outs = jnp.concatenate(
        [out_heads.reshape(tok_rows, q_cols), grad_query.reshape(tok_rows, q_cols)], axis=1
    )
    outs = lax.all_to_all(outs[:, None, :], GROUP, split_axis=0, concat_axis=1, tiled=True)
    kv_back = lax.all_to_all(kv_total[:, None, :], GROUP, split_axis=0, concat_axis=1, tiled=True)
    attended = outs[:, :, :q_cols].reshape(tok_dev, -1)
    grad_queries = outs[:, :, q_cols:].reshape(tok_dev, -1)
    grad_keys = kv_back[:, :, :kv_cols].reshape(tok_dev, -1)
    grad_values = kv_back[:, :, kv_cols:].reshape(tok_dev, -1)
    return (attended, grad_queries, grad_keys, grad_values)


def solution(mesh):
    n_seq = mesh.shape["seq"]
    n_tp = mesh.shape["tp"]
    split_mesh = Mesh(
        mesh.devices.reshape(n_seq // 2, 2, n_tp), ("chip", "core", "tp")
    )
    rows = P(("chip", "core", "tp"), None)
    in_specs = (rows, rows, rows, rows, P(("chip", "core")))
    out_specs = (rows, rows, rows, rows)
    return jax.shard_map(
        per_device, mesh=split_mesh, in_specs=in_specs, out_specs=out_specs, check_vma=False
    )
```
